256 devices in a mesh: expert: 32 (over z_lo, x, core), replica: 8 (over z_hi, y).
Axes of the slice: x: 4, y: 4, z: 8 (z_hi: 2, z_lo: 4; z = z_hi * 4 + z_lo), core: 2. Of those that a mesh axis runs over, the one named last changes fastest.
Arguments:
- tokens: bfloat16 [2048, 4096], P(('expert', 'replica')), may hold values from -6 to 6
- expert_ids: int32 [2048, 8], P(('expert', 'replica')), may hold values from 0 to 31, as said below
- gate_weights: float32 [2048, 8], P(('expert', 'replica')), may hold values from 0.1 to 1
- expert_holder: int32 [32], replicated, may hold values from 0 to 31, each once
- swap_pairs: int32 [8, 2], replicated, may hold values from 0 to 31, as said below
- capacity: int32 [32], replicated, may hold values from 2 to 4, as said below
- w_gate: bfloat16 [32, 1536, 4096], P('expert', 'replica'), may hold values from -0.09375 to 0.09375
- w_up: bfloat16 [32, 1536, 4096], P('expert', 'replica'), may hold values from -0.09375 to 0.09375
- w_down: bfloat16 [32, 1536, 4096], P('expert', 'replica'), may hold values from -0.15625 to 0.15625
Outputs:
- moe_output: bfloat16 [2048, 4096], P(('expert', 'replica'))
- moved_gate: bfloat16 [32, 1536, 4096], P('expert', 'replica')
- moved_up: bfloat16 [32, 1536, 4096], P('expert', 'replica')
- moved_down: bfloat16 [32, 1536, 4096], P('expert', 'replica')
- expert_peak: float32 [32], P('expert')
The draws below stay inside these ranges and needn't reach their ends.
Inputs may be any that keep to these rules, and one draw needn't show every extreme that they name: `expert_ids`: each token names 8 different experts; among one device's 8 tokens no expert is named more than 4 times, and one expert is named exactly 4 times by the tokens of every device. `swap_pairs`: no index appears twice; the two indices of every pair differ by 16. The expert named 4 times by every device has capacity 4. `expert_holder`: each index of the expert axis holds one expert.
All inputs are finite; a program needn't handle non-finite values.
Results may differ from the reference program's by a relative error of at most 0.014.
Values may be sent and summed in bfloat16 or wider, within the bound.
No kernel may reach another device: no remote copies, remote signals or barrier semaphores. Data moves between devices by JAX's collectives and lax.ppermute only.
A program may use at most 128 MiB of HBM per device.

```python
import math
import jax
import jax.numpy as jnp
from jax import lax

D = 4096
FF = 1536
TOPK = 8
TOK_DEV = 8
CAP = 4
EXPERTS = 32
FFD = 192
PAIRS = 8
TOKENS = 2048
N_REPLICA = 8


def hot_expert(key):
    return jax.random.randint(jax.random.fold_in(key, 7), (), 0, EXPERTS)


def draw_expert_ids(key, part):
    favored = hot_expert(key)
    blocks = TOKENS // TOK_DEV
    block_keys = jax.random.split(jax.random.fold_in(key, 11), blocks)

    def one_block(block_key):
        first_key, second_key = jax.random.split(block_key)
        ordering = jax.random.permutation(first_key, EXPERTS)
        where_hot = jnp.argmax(ordering == favored)
        hot_spot = TOK_DEV - 1
        ordering = ordering.at[where_hot].set(ordering[hot_spot]).at[hot_spot].set(favored)
        offsets = jax.random.permutation(second_key, TOK_DEV)
        spots = (offsets[:, None] + 2 * jnp.arange(TOPK)[None, :]) % EXPERTS
        return ordering[spots]
    return jax.vmap(one_block)(block_keys).reshape(TOKENS, TOPK).astype(jnp.int32)


def draw_capacity(key, part):
    favored = hot_expert(key)
    limits = jax.random.randint(jax.random.fold_in(key, 13), (EXPERTS,), CAP // 2, CAP + 1)
    return limits.at[favored].set(CAP).astype(jnp.int32)


def draw_swap_pairs(key, part):
    half = EXPERTS // 2
    lower = jax.random.permutation(jax.random.fold_in(key, 17), half)[0:PAIRS]
    flipped = jax.random.randint(jax.random.fold_in(key, 19), (PAIRS,), 0, 2)
    upper = lower + half
    first_dev = jnp.where(flipped == 1, upper, lower)
    second_dev = jnp.where(flipped == 1, lower, upper)
    return jnp.stack([first_dev, second_dev], axis=1).astype(jnp.int32)


def level_of(stream_key, dims, pieces, low, high):
    factor_of, own = 1.0, jax.random.fold_in(stream_key, 6)
    for position, parts in pieces:
        steps = jnp.exp(jax.random.uniform(jax.random.fold_in(own, position), (parts,), jnp.float32, low / len(pieces), high / len(pieces)))
        factor_of = factor_of * jnp.repeat(steps, dims[position] // parts).reshape([-1 if axis == position else 1 for axis in range(len(dims))])
    return factor_of


def normal_values(key, extent, deviation, reach, pieces=(), kind=jnp.bfloat16):
    loudness = level_of(key, extent, pieces, -0.22, 0.18) if pieces else 1.0
    drawn = jax.random.normal(key, extent, jnp.float32) * deviation * loudness
    return jnp.minimum(jnp.maximum(drawn, -reach), reach).astype(kind)


def setup_inputs(seed: int = 0) -> dict:
    streams_of = jax.random.split(jax.random.key(seed), 10)
    tokens = normal_values(streams_of[0], (TOKENS, D), 1.0, 6.0, ((0, 256),))
    expert_ids = draw_expert_ids(jax.random.fold_in(streams_of[9], 71), 0)
    gate_weights = jnp.clip(jnp.exp(math.log(1.0) - 2.3025851 * jax.random.uniform(streams_of[2], (TOKENS, TOPK), jnp.float32) ** level_of(streams_of[2], (TOKENS, TOPK), ((0, 256),), -0.2, 0.2)), 0.1, 1.0)
    expert_holder = jax.random.permutation(streams_of[3], EXPERTS).astype(jnp.int32)
    swap_pairs = draw_swap_pairs(jax.random.fold_in(streams_of[9], 71), 0)
    capacity = draw_capacity(jax.random.fold_in(streams_of[9], 71), 0)
    w_gate = normal_values(streams_of[6], (EXPERTS, FF, D), D ** -0.5, 0.09375, ((0, 32), (1, 8)))
    w_up = normal_values(streams_of[7], (EXPERTS, FF, D), D ** -0.5, 0.09375, ((0, 32), (1, 8)))
    w_down = normal_values(streams_of[8], (EXPERTS, FF, D), FF ** -0.5, 0.15625, ((0, 32), (1, 8)))
    return dict(tokens=tokens, expert_ids=expert_ids, gate_weights=gate_weights, expert_holder=expert_holder, swap_pairs=swap_pairs, capacity=capacity, w_gate=w_gate, w_up=w_up, w_down=w_down)


def pair_partner(swap_pairs):
    devices = jnp.arange(EXPERTS, dtype=jnp.int32)
    first_dev = swap_pairs[:, 0:1]
    second_dev = swap_pairs[:, 1:2]
    offsets = jnp.where(devices[None, :] == first_dev, second_dev - first_dev, 0)
    offsets = offsets + jnp.where(devices[None, :] == second_dev, first_dev - second_dev, 0)
    return (devices + jnp.sum(offsets, axis=0)).astype(jnp.int32)


def reference(tokens, expert_ids, gate_weights, expert_holder, swap_pairs, capacity, w_gate, w_up, w_down):
    partner = pair_partner(swap_pairs)
    moved_gate = w_gate[partner]
    moved_up = w_up[partner]
    moved_down = w_down[partner]
    holder_after = partner[expert_holder]
    blocks = TOKENS // TOK_DEV
    per_block = TOK_DEV * TOPK
    block_ids = expert_ids.reshape(blocks, per_block)
    chosen = (block_ids[:, :, None] == jnp.arange(EXPERTS, dtype=jnp.int32)[None, None, :]).astype(jnp.int32)
    earlier = jnp.cumsum(chosen, axis=1).astype(jnp.int32) - chosen
    ranking = jnp.sum(earlier * chosen, axis=2).astype(jnp.int32)
    slot_kept = ranking < capacity[block_ids]
    owners = (jnp.arange(blocks, dtype=jnp.int32)[:, None] * TOK_DEV
              + jnp.arange(per_block, dtype=jnp.int32)[None, :] // TOPK).astype(jnp.int32)
    scales = jnp.where(slot_kept, gate_weights.reshape(blocks, per_block), jnp.float32(0.0))
    levels = jnp.arange(CAP, dtype=jnp.int32)

    def one_expert(carried, expert):
        totals, peak_values = carried
        wanted = slot_kept & (block_ids == expert)
        matched = wanted[:, None, :] & (ranking[:, None, :] == levels[None, :, None])
        filled = jnp.any(matched, axis=2).reshape(-1)
        row_index = jnp.sum(jnp.where(matched, owners[:, None, :], 0), axis=2).astype(jnp.int32).reshape(-1)
        factor = jnp.sum(jnp.where(matched, scales[:, None, :], jnp.float32(0.0)), axis=2).reshape(-1)
        rows_in = jnp.where(filled[:, None], tokens[row_index], jnp.zeros((), tokens.dtype))
        holder = expert_holder[expert]
        gate_value = jnp.dot(rows_in, w_gate[holder].T, preferred_element_type=jnp.float32)
        up_value = jnp.dot(rows_in, w_up[holder].T, preferred_element_type=jnp.float32)
        hidden = (jax.nn.silu(gate_value) * up_value).astype(jnp.bfloat16)
        down_block = w_down[holder]
        summed = jnp.zeros((rows_in.shape[0], D), jnp.float32)
        for part_index in range(N_REPLICA):
            lower_unit = part_index * FFD
            partial_value = jnp.dot(hidden[:, lower_unit:lower_unit + FFD], down_block[lower_unit:lower_unit + FFD, :],
                              preferred_element_type=jnp.float32)
            summed = summed + lax.optimization_barrier(partial_value.astype(jnp.bfloat16)).astype(jnp.float32)
        result = lax.optimization_barrier(summed.astype(jnp.bfloat16)).astype(jnp.float32)
        totals = totals.at[row_index].add(result * factor[:, None])
        peak_values = peak_values.at[holder_after[expert]].set(jnp.max(jnp.abs(hidden)).astype(jnp.float32))
        return (totals, peak_values), None

    initial = (jnp.zeros((TOKENS, D), jnp.float32), jnp.zeros((EXPERTS,), jnp.float32))
    scanned = lax.scan(one_expert, initial, jnp.arange(EXPERTS, dtype=jnp.int32))
    totals, peak_values = scanned[0]
    return totals.astype(jnp.bfloat16), moved_gate, moved_up, moved_down, peak_values
```

```python
import jax
import jax.numpy as jnp
from jax import lax
from jax.sharding import PartitionSpec as P

TOPK = 8
CAP = 4


def pair_partner(swap_pairs, device_count):
    devices = jnp.arange(device_count, dtype=jnp.int32)
    first_dev = swap_pairs[:, 0:1]
    second_dev = swap_pairs[:, 1:2]
    offsets = jnp.where(devices[None, :] == first_dev, second_dev - first_dev, 0)
    offsets = offsets + jnp.where(devices[None, :] == second_dev, first_dev - second_dev, 0)
    return devices + jnp.sum(offsets, axis=0)


def table_lookup(values_table, positions):
    matches = positions[..., None] == jnp.arange(values_table.shape[0], dtype=jnp.int32)
    return jnp.sum(jnp.where(matches, values_table, 0), axis=-1)


def route_slots(expert_ids, holder_now, capacity):
    expert_count = holder_now.shape[0]
    flat_ids = expert_ids.reshape(-1)
    chosen = (flat_ids[:, None] == jnp.arange(expert_count, dtype=jnp.int32)[None, :]).astype(
        jnp.int32
    )
    earlier = jnp.cumsum(chosen, axis=0) - chosen
    ranking = jnp.sum(earlier * chosen, axis=1)
    slot_kept = ranking < table_lookup(capacity, flat_ids)
    target = table_lookup(holder_now, flat_ids)
    slot_ids = jnp.where(slot_kept, target * CAP + ranking, -1)
    matched = slot_ids[None, :] == jnp.arange(expert_count * CAP, dtype=jnp.int32)[:, None]
    owners = jnp.arange(flat_ids.shape[0], dtype=jnp.int32) // TOPK
    source = jnp.sum(jnp.where(matched, owners[None, :], 0), axis=1)
    filled = jnp.any(matched, axis=1)
    return (jnp.maximum(slot_ids, 0), slot_kept, source, filled)


def expert_hidden(row_block, gate_local, up_local):
    leading = row_block.shape[:-1]
    row_matrix = row_block.reshape(-1, row_block.shape[-1])
    contract = (((1,), (1,)), ((), ()))
    gate_value = lax.dot_general(
        row_matrix, gate_local, contract, preferred_element_type=jnp.float32
    )
    up_value = lax.dot_general(row_matrix, up_local, contract, preferred_element_type=jnp.float32)
    hidden = (jax.nn.silu(gate_value) * up_value).astype(jnp.bfloat16)
    return hidden.reshape(leading + (gate_local.shape[0],))


def shards(
    tokens, expert_ids, gate_weights, expert_holder, swap_pairs, capacity, w_gate, w_up, w_down
):
    experts = lax.axis_size("expert")
    replicas = lax.axis_size("replica")
    tok_rows, width = tokens.shape
    partner = pair_partner(swap_pairs, experts)
    me = lax.axis_index("expert")
    swapped = lax.dynamic_index_in_dim(partner, me, 0, keepdims=False) != me
    half = experts // 2
    ring = [(d, (d + half) % experts) for d in range(experts)]
    arrived = tuple(lax.ppermute(w, "expert", ring) for w in (w_gate, w_up, w_down))
    moved_gate, moved_up, moved_down = (
        jnp.where(swapped, got, own) for got, own in zip(arrived, (w_gate, w_up, w_down))
    )
    gate_local, up_local, down_local = (w_gate[0], w_up[0], w_down[0])
    group_tokens, group_ids = (
        lax.all_gather(tokens, "replica", axis=0, tiled=True),
        lax.all_gather(expert_ids, "replica", axis=0, tiled=True),
    )
    group_ids = group_ids.reshape(replicas, tok_rows, TOPK)
    slot_all, kept_all, source_all, filled_all = jax.vmap(route_slots, in_axes=(0, None, None))(
        group_ids, expert_holder, capacity
    )
    starts = jnp.arange(replicas, dtype=jnp.int32)[:, None] * tok_rows
    picked = jnp.take(group_tokens, source_all + starts, axis=0)
    outgoing = jnp.where(filled_all[:, :, None], picked, jnp.zeros((), jnp.bfloat16))
    hidden = expert_hidden(
        lax.all_to_all(
            outgoing.reshape(replicas, experts, CAP, width),
            "expert",
            split_axis=1,
            concat_axis=1,
            tiled=True,
        ),
        gate_local,
        up_local,
    )
    replica_index = lax.axis_index("replica")
    slot_of = lax.dynamic_index_in_dim(slot_all, replica_index, 0, keepdims=False)
    slot_kept = lax.dynamic_index_in_dim(kept_all, replica_index, 0, keepdims=False)
    hidden_rows = hidden.reshape(-1, hidden.shape[-1])
    local_peak = jnp.max(jnp.abs(hidden_rows)).astype(jnp.float32)
    summed = lax.psum_scatter(
        jnp.dot(hidden_rows, down_local, preferred_element_type=jnp.float32).astype(jnp.bfloat16),
        "replica",
        scatter_dimension=0,
        tiled=True,
    )
    results = summed.reshape(experts, CAP, width)
    returned = lax.all_to_all(results, "expert", split_axis=0, concat_axis=0, tiled=True)
    fetched = jnp.take(returned.reshape(experts * CAP, width), slot_of, axis=0).reshape(
        tok_rows, TOPK, width
    )
    scales = jnp.where(slot_kept, gate_weights.reshape(-1), jnp.float32(0.0)).reshape(
        tok_rows, TOPK, 1
    )
    moe_output = jnp.sum(scales * fetched, axis=1).astype(jnp.bfloat16)
    group_peak = lax.pmax(local_peak, "replica")
    expert_peak = jnp.where(swapped, lax.ppermute(group_peak, "expert", ring), group_peak)
    return (moe_output, moved_gate, moved_up, moved_down, expert_peak.reshape(1))


def solution(mesh):
    placed = (
        P(("expert", "replica"), None),
        P(("expert", "replica"), None),
        P(("expert", "replica"), None),
        P(),
        P(),
        P(),
        P("expert", "replica", None),
        P("expert", "replica", None),
        P("expert", "replica", None),
    )
    return jax.shard_map(
        shards,
        mesh=mesh,
        in_specs=placed,
        out_specs=(
            P(("expert", "replica"), None),
            P("expert", "replica", None),
            P("expert", "replica", None),
            P("expert", "replica", None),
            P("expert"),
        ),
        check_vma=False,
    )
```

```python
import jax
import jax.numpy as jnp
from jax import lax
from jax.sharding import PartitionSpec as P

TOPK = 8
CAP = 4


def pair_partner(swap_pairs, device_count):
    devices = jnp.arange(device_count, dtype=jnp.int32)
    first_dev = swap_pairs[:, 0:1]
    second_dev = swap_pairs[:, 1:2]
    offsets = jnp.where(devices[None, :] == first_dev, second_dev - first_dev, 0)
    offsets = offsets + jnp.where(devices[None, :] == second_dev, first_dev - second_dev, 0)
    return devices + jnp.sum(offsets, axis=0)


def table_lookup(values_table, positions):
    matches = positions[..., None] == jnp.arange(values_table.shape[0], dtype=jnp.int32)
    return jnp.sum(jnp.where(matches, values_table, 0), axis=-1)


def route_slots(expert_ids, holder_now, capacity):
    expert_count = holder_now.shape[0]
    flat_ids = expert_ids.reshape(-1)
    chosen = (flat_ids[:, None] == jnp.arange(expert_count, dtype=jnp.int32)[None, :]).astype(
        jnp.int32
    )
    earlier = jnp.cumsum(chosen, axis=0) - chosen
    ranking = jnp.sum(earlier * chosen, axis=1)
    slot_kept = ranking < table_lookup(capacity, flat_ids)
    target = table_lookup(holder_now, flat_ids)
    slot_ids = jnp.where(slot_kept, target * CAP + ranking, -1)
    matched = slot_ids[None, :] == jnp.arange(expert_count * CAP, dtype=jnp.int32)[:, None]
    owners = jnp.arange(flat_ids.shape[0], dtype=jnp.int32) // TOPK
    source = jnp.sum(jnp.where(matched, owners[None, :], 0), axis=1)
    filled = jnp.any(matched, axis=1)
    return (jnp.maximum(slot_ids, 0), slot_kept, source, filled)


def expert_hidden(row_block, gate_local, up_local):
    leading = row_block.shape[:-1]
    row_matrix = row_block.reshape(-1, row_block.shape[-1])
    contract = (((1,), (1,)), ((), ()))
    gate_value = lax.dot_general(
        row_matrix, gate_local, contract, preferred_element_type=jnp.float32
    )
    up_value = lax.dot_general(row_matrix, up_local, contract, preferred_element_type=jnp.float32)
    hidden = (jax.nn.silu(gate_value) * up_value).astype(jnp.bfloat16)
    return hidden.reshape(leading + (gate_local.shape[0],))


def shards(
    tokens, expert_ids, gate_weights, expert_holder, swap_pairs, capacity, w_gate, w_up, w_down
):
    experts = lax.axis_size("expert")
    replicas = lax.axis_size("replica")
    tok_rows, width = tokens.shape
    units = w_gate.shape[1]
    cols = width // replicas
    partner = pair_partner(swap_pairs, experts)
    me = lax.axis_index("expert")
    swapped = lax.dynamic_index_in_dim(partner, me, 0, keepdims=False) != me
    half = experts // 2
    ring = [(d, (d + half) % experts) for d in range(experts)]
    arrived = tuple(lax.ppermute(w, "expert", ring) for w in (w_gate, w_up, w_down))
    down_cols = lax.all_to_all(
        w_down[0].reshape(units, replicas, cols),
        "replica",
        split_axis=1,
        concat_axis=0,
        tiled=True,
    ).reshape(units * replicas, cols)
    slot_of, slot_kept, source, filled = route_slots(expert_ids, expert_holder, capacity)
    outgoing = jnp.where(
        filled[:, None], jnp.take(tokens, source, axis=0), jnp.zeros((), jnp.bfloat16)
    )
    arrived_rows = lax.all_to_all(outgoing.reshape(experts, CAP, width), "expert", 0, 0, tiled=True)
    group_rows = lax.all_gather(arrived_rows, "replica", axis=0, tiled=False)
    hidden = expert_hidden(group_rows, w_gate[0], w_up[0]).reshape(-1, units)
    hidden_all = lax.all_gather(hidden, "replica", axis=1, tiled=True)
    group_peak = jnp.max(jnp.abs(hidden_all)).astype(jnp.float32)
    out_cols = jnp.dot(
        hidden_all, down_cols, preferred_element_type=jnp.float32
    ).astype(jnp.bfloat16)
    full_rows = lax.all_to_all(
        out_cols.reshape(replicas, experts, CAP, cols),
        "replica",
        split_axis=0,
        concat_axis=3,
        tiled=True,
    )
    returned = lax.all_to_all(full_rows.reshape(experts, CAP, width), "expert", 0, 0, tiled=True)
    fetched = jnp.take(returned.reshape(experts * CAP, width), slot_of, axis=0).reshape(
        tok_rows, TOPK, width
    )
    scales = jnp.where(slot_kept, gate_weights.reshape(-1), jnp.float32(0.0)).reshape(
        tok_rows, TOPK, 1
    )
    moe_output = jnp.sum(scales * fetched, axis=1).astype(jnp.bfloat16)
    moved_gate, moved_up, moved_down = (
        jnp.where(swapped, got, own) for got, own in zip(arrived, (w_gate, w_up, w_down))
    )
    expert_peak = jnp.where(swapped, lax.ppermute(group_peak, "expert", ring), group_peak)
    return (moe_output, moved_gate, moved_up, moved_down, expert_peak.reshape(1))


def solution(mesh):
    placed = (
        P(("expert", "replica"), None),
        P(("expert", "replica"), None),
        P(("expert", "replica"), None),
        P(),
        P(),
        P(),
        P("expert", "replica", None),
        P("expert", "replica", None),
        P("expert", "replica", None),
    )
    return jax.shard_map(
        shards,
        mesh=mesh,
        in_specs=placed,
        out_specs=(
            P(("expert", "replica"), None),
            P("expert", "replica", None),
            P("expert", "replica", None),
            P("expert", "replica", None),
            P("expert"),
        ),
        check_vma=False,
    )
```

```python
import jax
import jax.numpy as jnp
from jax import lax
from jax.sharding import PartitionSpec as P

TOPK = 8
CAP = 4
HALVES = 2


def pair_partner(swap_pairs, device_count):
    devices = jnp.arange(device_count, dtype=jnp.int32)
    first_dev = swap_pairs[:, 0:1]
    second_dev = swap_pairs[:, 1:2]
    offsets = jnp.where(devices[None, :] == first_dev, second_dev - first_dev, 0)
    offsets = offsets + jnp.where(devices[None, :] == second_dev, first_dev - second_dev, 0)
    return devices + jnp.sum(offsets, axis=0)


def table_lookup(values_table, positions):
    matches = positions[..., None] == jnp.arange(values_table.shape[0], dtype=jnp.int32)
    return jnp.sum(jnp.where(matches, values_table, 0), axis=-1)


def route_slots(expert_ids, holder_now, capacity):
    expert_count = holder_now.shape[0]
    flat_ids = expert_ids.reshape(-1)
    chosen = (flat_ids[:, None] == jnp.arange(expert_count, dtype=jnp.int32)[None, :]).astype(
        jnp.int32
    )
    earlier = jnp.cumsum(chosen, axis=0) - chosen
    ranking = jnp.sum(earlier * chosen, axis=1)
    slot_kept = ranking < table_lookup(capacity, flat_ids)
    target = table_lookup(holder_now, flat_ids)
    slot_ids = jnp.where(slot_kept, target * CAP + ranking, -1)
    matched = slot_ids[None, :] == jnp.arange(expert_count * CAP, dtype=jnp.int32)[:, None]
    owners = jnp.arange(flat_ids.shape[0], dtype=jnp.int32) // TOPK
    source = jnp.sum(jnp.where(matched, owners[None, :], 0), axis=1)
    filled = jnp.any(matched, axis=1)
    return (jnp.maximum(slot_ids, 0), slot_kept, source, filled)


def expert_hidden(row_block, gate_local, up_local):
    leading = row_block.shape[:-1]
    row_matrix = row_block.reshape(-1, row_block.shape[-1])
    contract = (((1,), (1,)), ((), ()))
    gate_value = lax.dot_general(
        row_matrix, gate_local, contract, preferred_element_type=jnp.float32
    )
    up_value = lax.dot_general(row_matrix, up_local, contract, preferred_element_type=jnp.float32)
    hidden = (jax.nn.silu(gate_value) * up_value).astype(jnp.bfloat16)
    return hidden.reshape(leading + (gate_local.shape[0],))


def canonical(mine, theirs, first):
    return jnp.stack([jnp.where(first, mine, theirs), jnp.where(first, theirs, mine)])


def shards(
    tokens, expert_ids, gate_weights, expert_holder, swap_pairs, capacity, w_gate, w_up, w_down
):
    experts = lax.axis_size("expert")
    replicas = lax.axis_size("replica")
    tok_rows, width = tokens.shape
    units = w_gate.shape[1]
    cols = width // replicas
    ys = replicas // HALVES
    partner = pair_partner(swap_pairs, experts)
    me = lax.axis_index("expert")
    swapped = lax.dynamic_index_in_dim(partner, me, 0, keepdims=False) != me
    half = experts // 2
    ring = [(d, (d + half) % experts) for d in range(experts)]
    rep = lax.axis_index("replica")
    zh = rep // ys
    first = zh == 0
    across = [(q, (q + ys) % replicas) for q in range(replicas)]
    ygroups = [[h * ys + j for j in range(ys)] for h in range(HALVES)]
    arrived = tuple(lax.ppermute(w, "expert", ring) for w in (w_gate, w_up, w_down))
    down_cols = lax.all_to_all(
        w_down[0].reshape(units, replicas, cols),
        "replica",
        split_axis=1,
        concat_axis=0,
        tiled=True,
    ).reshape(replicas, units, cols)
    blk_tokens = canonical(tokens, lax.ppermute(tokens, "replica", across), first)
    blk_ids = canonical(expert_ids, lax.ppermute(expert_ids, "replica", across), first)
    blk_gw = canonical(gate_weights, lax.ppermute(gate_weights, "replica", across), first)
    slot_of, slot_kept, source, filled = jax.vmap(route_slots, in_axes=(0, None, None))(
        blk_ids, expert_holder, capacity
    )
    picked = jax.vmap(lambda t, s: jnp.take(t, s, axis=0))(blk_tokens, source)
    outgoing = jnp.where(filled[..., None], picked, jnp.zeros((), jnp.bfloat16))
    outgoing = outgoing.reshape(HALVES, experts, CAP, width).transpose(1, 0, 2, 3)
    arrived_rows = lax.all_to_all(outgoing, "expert", 0, 0, tiled=True)
    group_rows = lax.all_gather(
        arrived_rows, "replica", axis=0, tiled=False, axis_index_groups=ygroups
    )
    hidden = expert_hidden(group_rows, w_gate[0], w_up[0]).reshape(-1, units)
    pair_hidden = canonical(hidden, lax.ppermute(hidden, "replica", across), first)
    hidden_all = lax.all_gather(
        pair_hidden, "replica", axis=1, tiled=False, axis_index_groups=ygroups
    ).reshape(replicas, -1, units)
    group_peak = jnp.max(jnp.abs(hidden_all)).astype(jnp.float32)
    out_cols = lax.dot_general(
        hidden_all,
        down_cols,
        (((0, 2), (0, 1)), ((), ())),
        preferred_element_type=jnp.float32,
    ).astype(jnp.bfloat16)
    half_rows = lax.all_to_all(
        out_cols.reshape(ys, experts, HALVES, CAP, cols),
        "replica",
        split_axis=0,
        concat_axis=4,
        tiled=True,
        axis_index_groups=ygroups,
    )
    returned = lax.all_to_all(
        half_rows.reshape(experts, HALVES, CAP, ys * cols), "expert", 0, 0, tiled=True
    )
    by_block = returned.transpose(1, 0, 2, 3).reshape(HALVES, experts * CAP, ys * cols)
    fetched = jax.vmap(lambda t, s: jnp.take(t, s, axis=0))(by_block, slot_of)
    scales = jnp.where(slot_kept, blk_gw.reshape(HALVES, -1), jnp.float32(0.0))
    combined = jnp.sum(
        (scales[..., None] * fetched).reshape(HALVES, tok_rows, TOPK, ys * cols), axis=2
    )
    own_half = jnp.where(first, combined[0], combined[1])
    send_half = jnp.where(first, combined[1], combined[0])
    recv_half = lax.ppermute(send_half, "replica", across)
    moe_output = jnp.where(
        first,
        jnp.concatenate([own_half, recv_half], axis=1),
        jnp.concatenate([recv_half, own_half], axis=1),
    ).astype(jnp.bfloat16)
    moved_gate, moved_up, moved_down = (
        jnp.where(swapped, got, own) for got, own in zip(arrived, (w_gate, w_up, w_down))
    )
    expert_peak = jnp.where(swapped, lax.ppermute(group_peak, "expert", ring), group_peak)
    return (moe_output, moved_gate, moved_up, moved_down, expert_peak.reshape(1))


def solution(mesh):
    placed = (
        P(("expert", "replica"), None),
        P(("expert", "replica"), None),
        P(("expert", "replica"), None),
        P(),
        P(),
        P(),
        P("expert", "replica", None),
        P("expert", "replica", None),
        P("expert", "replica", None),
    )
    return jax.shard_map(
        shards,
        mesh=mesh,
        in_specs=placed,
        out_specs=(
            P(("expert", "replica"), None),
            P("expert", "replica", None),
            P("expert", "replica", None),
            P("expert", "replica", None),
            P("expert"),
        ),
        check_vma=False,
    )
```

```python
import jax
import jax.numpy as jnp
from jax import lax
from jax.sharding import PartitionSpec as P

TOPK = 8
CAP = 4
HALVES = 2
PLANES = 4


def pair_partner(swap_pairs, device_count):
    devices = jnp.arange(device_count, dtype=jnp.int32)
    first_dev = swap_pairs[:, 0:1]
    second_dev = swap_pairs[:, 1:2]
    offsets = jnp.where(devices[None, :] == first_dev, second_dev - first_dev, 0)
    offsets = offsets + jnp.where(devices[None, :] == second_dev, first_dev - second_dev, 0)
    return devices + jnp.sum(offsets, axis=0)


def table_lookup(values_table, positions):
    matches = positions[..., None] == jnp.arange(values_table.shape[0], dtype=jnp.int32)
    return jnp.sum(jnp.where(matches, values_table, 0), axis=-1)


def route_slots(expert_ids, holder_now, capacity):
    expert_count = holder_now.shape[0]
    flat_ids = expert_ids.reshape(-1)
    chosen = (flat_ids[:, None] == jnp.arange(expert_count, dtype=jnp.int32)[None, :]).astype(
        jnp.int32
    )
    earlier = jnp.cumsum(chosen, axis=0) - chosen
    ranking = jnp.sum(earlier * chosen, axis=1)
    slot_kept = ranking < table_lookup(capacity, flat_ids)
    target = table_lookup(holder_now, flat_ids)
    slot_ids = jnp.where(slot_kept, target * CAP + ranking, -1)
    matched = slot_ids[None, :] == jnp.arange(expert_count * CAP, dtype=jnp.int32)[:, None]
    owners = jnp.arange(flat_ids.shape[0], dtype=jnp.int32) // TOPK
    source = jnp.sum(jnp.where(matched, owners[None, :], 0), axis=1)
    filled = jnp.any(matched, axis=1)
    return (jnp.maximum(slot_ids, 0), slot_kept, source, filled)


def expert_hidden(row_block, gate_local, up_local):
    leading = row_block.shape[:-1]
    row_matrix = row_block.reshape(-1, row_block.shape[-1])
    contract = (((1,), (1,)), ((), ()))
    gate_value = lax.dot_general(
        row_matrix, gate_local, contract, preferred_element_type=jnp.float32
    )
    up_value = lax.dot_general(row_matrix, up_local, contract, preferred_element_type=jnp.float32)
    hidden = (jax.nn.silu(gate_value) * up_value).astype(jnp.bfloat16)
    return hidden.reshape(leading + (gate_local.shape[0],))


def canonical(mine, theirs, first):
    return jnp.stack([jnp.where(first, mine, theirs), jnp.where(first, theirs, mine)])


def shards(
    tokens, expert_ids, gate_weights, expert_holder, swap_pairs, capacity, w_gate, w_up, w_down
):
    experts = lax.axis_size("expert")
    replicas = lax.axis_size("replica")
    tok_rows, width = tokens.shape
    units = w_gate.shape[1]
    cols = width // replicas
    ys = replicas // HALVES
    plane = experts // PLANES
    blocks = PLANES * HALVES
    partner = pair_partner(swap_pairs, experts)
    me = lax.axis_index("expert")
    zl = me // plane
    swapped = lax.dynamic_index_in_dim(partner, me, 0, keepdims=False) != me
    half = experts // 2
    ring = [(d, (d + half) % experts) for d in range(experts)]
    rep = lax.axis_index("replica")
    zh = rep // ys
    first = zh == 0
    across = [(q, (q + ys) % replicas) for q in range(replicas)]
    ygroups = [[h * ys + j for j in range(ys)] for h in range(HALVES)]
    zgroups = [[p * plane + c for p in range(PLANES)] for c in range(plane)]
    pgroups = [[p * plane + c for c in range(plane)] for p in range(PLANES)]
    arrived = tuple(lax.ppermute(w, "expert", ring) for w in (w_gate, w_up, w_down))
    down_cols = lax.all_to_all(
        w_down[0].reshape(units, replicas, cols),
        "replica",
        split_axis=1,
        concat_axis=0,
        tiled=True,
    ).reshape(replicas, units, cols)
    pair_tokens = canonical(tokens, lax.ppermute(tokens, "replica", across), first)
    pair_ids = canonical(expert_ids, lax.ppermute(expert_ids, "replica", across), first)
    pair_gw = canonical(gate_weights, lax.ppermute(gate_weights, "replica", across), first)
    blk_tokens, blk_ids, blk_gw = (
        lax.all_gather(v, "expert", axis=0, tiled=True, axis_index_groups=zgroups)
        for v in (pair_tokens, pair_ids, pair_gw)
    )
    slot_of, slot_kept, source, filled = jax.vmap(route_slots, in_axes=(0, None, None))(
        blk_ids, expert_holder, capacity
    )
    lo = zl * (plane * CAP)
    source = lax.dynamic_slice_in_dim(source, lo, plane * CAP, axis=1)
    filled = lax.dynamic_slice_in_dim(filled, lo, plane * CAP, axis=1)
    picked = jax.vmap(lambda t, s: jnp.take(t, s, axis=0))(blk_tokens, source)
    outgoing = jnp.where(filled[..., None], picked, jnp.zeros((), jnp.bfloat16))
    outgoing = outgoing.reshape(blocks, plane, CAP, width).transpose(1, 0, 2, 3)
    arrived_rows = lax.all_to_all(
        outgoing.reshape(plane, blocks * CAP, width),
        "expert",
        0,
        0,
        tiled=True,
        axis_index_groups=pgroups,
    )
    group_rows = lax.all_gather(
        arrived_rows, "replica", axis=0, tiled=False, axis_index_groups=ygroups
    )
    hidden = expert_hidden(group_rows, w_gate[0], w_up[0]).reshape(-1, units)
    pair_hidden = canonical(hidden, lax.ppermute(hidden, "replica", across), first)
    hidden_all = lax.all_gather(
        pair_hidden, "replica", axis=1, tiled=False, axis_index_groups=ygroups
    ).reshape(replicas, -1, units)
    group_peak = jnp.max(jnp.abs(hidden_all)).astype(jnp.float32)
    out_cols = lax.dot_general(
        hidden_all,
        down_cols,
        (((0, 2), (0, 1)), ((), ())),
        preferred_element_type=jnp.float32,
    ).astype(jnp.bfloat16)
    half_rows = lax.all_to_all(
        out_cols.reshape(ys, plane, blocks * CAP, cols),
        "replica",
        split_axis=0,
        concat_axis=3,
        tiled=True,
        axis_index_groups=ygroups,
    )
    returned = lax.all_to_all(
        half_rows.reshape(plane, blocks * CAP, ys * cols),
        "expert",
        0,
        0,
        tiled=True,
        axis_index_groups=pgroups,
    )
    by_block = returned.reshape(plane, blocks, CAP, ys * cols).transpose(1, 0, 2, 3)
    by_block = by_block.reshape(blocks, plane * CAP, ys * cols)
    in_plane = (slot_of // (plane * CAP)) == zl
    local_slot = slot_of % (plane * CAP)
    fetched = jax.vmap(lambda t, s: jnp.take(t, s, axis=0))(by_block, local_slot)
    scales = jnp.where(slot_kept & in_plane, blk_gw.reshape(blocks, -1), jnp.float32(0.0))
    partial_sum = jnp.sum(
        (scales[..., None] * fetched).reshape(blocks, tok_rows, TOPK, ys * cols), axis=2
    )
    summed = lax.all_to_all(
        partial_sum.reshape(PLANES, HALVES, tok_rows, ys * cols),
        "expert",
        0,
        0,
        tiled=True,
        axis_index_groups=zgroups,
    )
    combined = jnp.sum(summed, axis=0)
    own_half = jnp.where(first, combined[0], combined[1])
    send_half = jnp.where(first, combined[1], combined[0])
    recv_half = lax.ppermute(send_half, "replica", across)
    moe_output = jnp.where(
        first,
        jnp.concatenate([own_half, recv_half], axis=1),
        jnp.concatenate([recv_half, own_half], axis=1),
    ).astype(jnp.bfloat16)
    moved_gate, moved_up, moved_down = (
        jnp.where(swapped, got, own) for got, own in zip(arrived, (w_gate, w_up, w_down))
    )
    expert_peak = jnp.where(swapped, lax.ppermute(group_peak, "expert", ring), group_peak)
    return (moe_output, moved_gate, moved_up, moved_down, expert_peak.reshape(1))


def solution(mesh):
    placed = (
        P(("expert", "replica"), None),
        P(("expert", "replica"), None),
        P(("expert", "replica"), None),
        P(),
        P(),
        P(),
        P("expert", "replica", None),
        P("expert", "replica", None),
        P("expert", "replica", None),
    )
    return jax.shard_map(
        shards,
        mesh=mesh,
        in_specs=placed,
        out_specs=(
            P(("expert", "replica"), None),
            P("expert", "replica", None),
            P("expert", "replica", None),
            P("expert", "replica", None),
            P("expert"),
        ),
        check_vma=False,
    )
```

```python
import jax
import jax.numpy as jnp
from jax import lax
from jax.sharding import PartitionSpec as P

TOPK = 8
CAP = 4
HALVES = 2


def pair_partner(swap_pairs, device_count):
    devices = jnp.arange(device_count, dtype=jnp.int32)
    first_dev = swap_pairs[:, 0:1]
    second_dev = swap_pairs[:, 1:2]
    offsets = jnp.where(devices[None, :] == first_dev, second_dev - first_dev, 0)
    offsets = offsets + jnp.where(devices[None, :] == second_dev, first_dev - second_dev, 0)
    return devices + jnp.sum(offsets, axis=0)


def table_lookup(values_table, positions):
    matches = positions[..., None] == jnp.arange(values_table.shape[0], dtype=jnp.int32)
    return jnp.sum(jnp.where(matches, values_table, 0), axis=-1)


def route_slots(expert_ids, holder_now, capacity):
    expert_count = holder_now.shape[0]
    flat_ids = expert_ids.reshape(-1)
    chosen = (flat_ids[:, None] == jnp.arange(expert_count, dtype=jnp.int32)[None, :]).astype(
        jnp.int32
    )
    earlier = jnp.cumsum(chosen, axis=0) - chosen
    ranking = jnp.sum(earlier * chosen, axis=1)
    slot_kept = ranking < table_lookup(capacity, flat_ids)
    target = table_lookup(holder_now, flat_ids)
    slot_ids = jnp.where(slot_kept, target * CAP + ranking, -1)
    matched = slot_ids[None, :] == jnp.arange(expert_count * CAP, dtype=jnp.int32)[:, None]
    owners = jnp.arange(flat_ids.shape[0], dtype=jnp.int32) // TOPK
    source = jnp.sum(jnp.where(matched, owners[None, :], 0), axis=1)
    filled = jnp.any(matched, axis=1)
    return (jnp.maximum(slot_ids, 0), slot_kept, source, filled)


def expert_hidden(row_block, gate_local, up_local):
    leading = row_block.shape[:-1]
    row_matrix = row_block.reshape(-1, row_block.shape[-1])
    contract = (((1,), (1,)), ((), ()))
    gate_value = lax.dot_general(
        row_matrix, gate_local, contract, preferred_element_type=jnp.float32
    )
    up_value = lax.dot_general(row_matrix, up_local, contract, preferred_element_type=jnp.float32)
    hidden = (jax.nn.silu(gate_value) * up_value).astype(jnp.bfloat16)
    return hidden.reshape(leading + (gate_local.shape[0],))


def canonical(mine, theirs, first):
    return jnp.stack([jnp.where(first, mine, theirs), jnp.where(first, theirs, mine)])


def shards(
    tokens, expert_ids, gate_weights, expert_holder, swap_pairs, capacity, w_gate, w_up, w_down
):
    experts = lax.axis_size("expert")
    replicas = lax.axis_size("replica")
    tok_rows, width = tokens.shape
    units = w_gate.shape[1]
    cols = width // replicas
    ys = replicas // HALVES
    partner = pair_partner(swap_pairs, experts)
    me = lax.axis_index("expert")
    swapped = lax.dynamic_index_in_dim(partner, me, 0, keepdims=False) != me
    half = experts // 2
    ring = [(d, (d + half) % experts) for d in range(experts)]
    rep = lax.axis_index("replica")
    zh = rep // ys
    first = zh == 0
    across = [(q, (q + ys) % replicas) for q in range(replicas)]
    ygroups = [[h * ys + j for j in range(ys)] for h in range(HALVES)]
    arrived = tuple(lax.ppermute(w, "expert", ring) for w in (w_gate, w_up, w_down))
    down_cols = lax.all_to_all(
        w_down[0].reshape(units, replicas, cols),
        "replica",
        split_axis=1,
        concat_axis=0,
        tiled=True,
    ).reshape(replicas, units, cols)
    blk_tokens = canonical(tokens, lax.ppermute(tokens, "replica", across), first)
    blk_ids = canonical(expert_ids, lax.ppermute(expert_ids, "replica", across), first)
    blk_gw = canonical(gate_weights, lax.ppermute(gate_weights, "replica", across), first)
    slot_of, slot_kept, source, filled = jax.vmap(route_slots, in_axes=(0, None, None))(
        blk_ids, expert_holder, capacity
    )
    picked = jax.vmap(lambda t, s: jnp.take(t, s, axis=0))(blk_tokens, source)
    outgoing = jnp.where(filled[..., None], picked, jnp.zeros((), jnp.bfloat16))
    outgoing = outgoing.reshape(HALVES, experts, CAP, width).transpose(1, 0, 2, 3)
    outgoing = outgoing.reshape(experts, HALVES * CAP, width)
    arrived_rows = lax.all_to_all(outgoing, "expert", 0, 0, tiled=True)
    group_rows = lax.all_gather(
        arrived_rows, "replica", axis=0, tiled=False, axis_index_groups=ygroups
    )
    hidden = expert_hidden(group_rows, w_gate[0], w_up[0]).reshape(-1, units)
    pair_hidden = canonical(hidden, lax.ppermute(hidden, "replica", across), first)
    hidden_all = lax.all_gather(
        pair_hidden, "replica", axis=0, tiled=False, axis_index_groups=ygroups
    )
    group_peak = jnp.max(jnp.abs(hidden_all)).astype(jnp.float32)
    expert_peak = jnp.where(swapped, lax.ppermute(group_peak, "expert", ring), group_peak)
    out_cols = lax.dot_general(
        hidden_all,
        down_cols.reshape(HALVES, ys, units, cols),
        (((0, 1, 3), (1, 0, 2)), ((), ())),
        preferred_element_type=jnp.float32,
    ).astype(jnp.bfloat16)
    half_rows = lax.all_to_all(
        out_cols.reshape(ys, experts, HALVES * CAP, cols),
        "replica",
        split_axis=0,
        concat_axis=3,
        tiled=True,
        axis_index_groups=ygroups,
    )
    returned = lax.all_to_all(
        half_rows.reshape(experts, HALVES * CAP, ys * cols), "expert", 0, 0, tiled=True
    ).reshape(experts, HALVES, CAP, ys * cols)
    by_block = returned.transpose(1, 0, 2, 3).reshape(HALVES, experts * CAP, ys * cols)
    fetched = jax.vmap(lambda t, s: jnp.take(t, s, axis=0))(by_block, slot_of)
    scales = jnp.where(slot_kept, blk_gw.reshape(HALVES, -1), jnp.float32(0.0))
    combined = jnp.sum(
        (scales[..., None] * fetched).reshape(HALVES, tok_rows, TOPK, ys * cols), axis=2
    )
    own_half = jnp.where(first, combined[0], combined[1])
    send_half = jnp.where(first, combined[1], combined[0])
    recv_half = lax.ppermute(send_half, "replica", across)
    moe_output = jnp.where(
        first,
        jnp.concatenate([own_half, recv_half], axis=1),
        jnp.concatenate([recv_half, own_half], axis=1),
    ).astype(jnp.bfloat16)
    moved_gate, moved_up, moved_down = (
        jnp.where(swapped, got, own) for got, own in zip(arrived, (w_gate, w_up, w_down))
    )
    return (moe_output, moved_gate, moved_up, moved_down, expert_peak.reshape(1))


def solution(mesh):
    placed = (
        P(("expert", "replica"), None),
        P(("expert", "replica"), None),
        P(("expert", "replica"), None),
        P(),
        P(),
        P(),
        P("expert", "replica", None),
        P("expert", "replica", None),
        P("expert", "replica", None),
    )
    return jax.shard_map(
        shards,
        mesh=mesh,
        in_specs=placed,
        out_specs=(
            P(("expert", "replica"), None),
            P("expert", "replica", None),
            P("expert", "replica", None),
            P("expert", "replica", None),
            P("expert"),
        ),
        check_vma=False,
    )
```

```python
import jax
import jax.numpy as jnp
from jax import lax
from jax.sharding import PartitionSpec as P

TOPK = 8
CAP = 4
HALVES = 2


def pair_partner(swap_pairs, device_count):
    devices = jnp.arange(device_count, dtype=jnp.int32)
    first_dev = swap_pairs[:, 0:1]
    second_dev = swap_pairs[:, 1:2]
    offsets = jnp.where(devices[None, :] == first_dev, second_dev - first_dev, 0)
    offsets = offsets + jnp.where(devices[None, :] == second_dev, first_dev - second_dev, 0)
    return devices + jnp.sum(offsets, axis=0)


def table_lookup(values_table, positions):
    matches = positions[..., None] == jnp.arange(values_table.shape[0], dtype=jnp.int32)
    return jnp.sum(jnp.where(matches, values_table, 0), axis=-1)


def route_slots(expert_ids, holder_now, capacity):
    expert_count = holder_now.shape[0]
    flat_ids = expert_ids.reshape(-1)
    chosen = (flat_ids[:, None] == jnp.arange(expert_count, dtype=jnp.int32)[None, :]).astype(
        jnp.int32
    )
    earlier = jnp.cumsum(chosen, axis=0) - chosen
    ranking = jnp.sum(earlier * chosen, axis=1)
    slot_kept = ranking < table_lookup(capacity, flat_ids)
    target = table_lookup(holder_now, flat_ids)
    slot_ids = jnp.where(slot_kept, target * CAP + ranking, -1)
    matched = slot_ids[None, :] == jnp.arange(expert_count * CAP, dtype=jnp.int32)[:, None]
    owners = jnp.arange(flat_ids.shape[0], dtype=jnp.int32) // TOPK
    source = jnp.sum(jnp.where(matched, owners[None, :], 0), axis=1)
    filled = jnp.any(matched, axis=1)
    return (jnp.maximum(slot_ids, 0), slot_kept, source, filled)


def expert_hidden(row_block, gate_local, up_local):
    leading = row_block.shape[:-1]
    row_matrix = row_block.reshape(-1, row_block.shape[-1])
    contract = (((1,), (1,)), ((), ()))
    gate_value = lax.dot_general(
        row_matrix, gate_local, contract, preferred_element_type=jnp.float32
    )
    up_value = lax.dot_general(row_matrix, up_local, contract, preferred_element_type=jnp.float32)
    hidden = (jax.nn.silu(gate_value) * up_value).astype(jnp.bfloat16)
    return hidden.reshape(leading + (gate_local.shape[0],))


def canonical(mine, theirs, first):
    return jnp.stack([jnp.where(first, mine, theirs), jnp.where(first, theirs, mine)])


def shards(
    tokens, expert_ids, gate_weights, expert_holder, swap_pairs, capacity, w_gate, w_up, w_down
):
    experts = lax.axis_size("expert")
    replicas = lax.axis_size("replica")
    tok_rows, width = tokens.shape
    units = w_gate.shape[1]
    cols = width // replicas
    ys = replicas // HALVES
    partner = pair_partner(swap_pairs, experts)
    me = lax.axis_index("expert")
    swapped = lax.dynamic_index_in_dim(partner, me, 0, keepdims=False) != me
    half = experts // 2
    ring = [(d, (d + half) % experts) for d in range(experts)]
    rep = lax.axis_index("replica")
    zh = rep // ys
    first = zh == 0
    across = [(q, (q + ys) % replicas) for q in range(replicas)]
    ygroups = [[h * ys + j for j in range(ys)] for h in range(HALVES)]
    arrived = tuple(lax.ppermute(w, "expert", ring) for w in (w_gate, w_up, w_down))
    down_cols = lax.all_to_all(
        w_down[0].reshape(units, replicas, cols),
        "replica",
        split_axis=1,
        concat_axis=0,
        tiled=True,
    ).reshape(replicas, units, cols)
    gw_hi = gate_weights.astype(jnp.bfloat16)
    gw_lo = (gate_weights - gw_hi.astype(jnp.float32)).astype(jnp.bfloat16)
    packed = jnp.concatenate([tokens, expert_ids.astype(jnp.bfloat16), gw_hi, gw_lo], axis=1)
    got = lax.ppermute(packed, "replica", across)
    their_ids = got[:, width : width + TOPK].astype(jnp.int32)
    their_gw = got[:, width + TOPK : width + 2 * TOPK].astype(jnp.float32) + got[
        :, width + 2 * TOPK :
    ].astype(jnp.float32)
    blk_tokens = canonical(tokens, got[:, :width], first)
    blk_ids = canonical(expert_ids, their_ids, first)
    blk_gw = canonical(gate_weights, their_gw, first)
    slot_of, slot_kept, source, filled = jax.vmap(route_slots, in_axes=(0, None, None))(
        blk_ids, expert_holder, capacity
    )
    picked = jax.vmap(lambda t, s: jnp.take(t, s, axis=0))(blk_tokens, source)
    outgoing = jnp.where(filled[..., None], picked, jnp.zeros((), jnp.bfloat16))
    outgoing = outgoing.reshape(HALVES, experts, CAP, width).transpose(1, 0, 2, 3)
    outgoing = outgoing.reshape(experts, HALVES * CAP, width)
    arrived_rows = lax.all_to_all(outgoing, "expert", 0, 0, tiled=True)
    group_rows = lax.all_gather(
        arrived_rows, "replica", axis=0, tiled=False, axis_index_groups=ygroups
    )
    hidden = expert_hidden(group_rows, w_gate[0], w_up[0]).reshape(-1, units)
    pair_hidden = canonical(hidden, lax.ppermute(hidden, "replica", across), first)
    hidden_all = lax.all_gather(
        pair_hidden, "replica", axis=0, tiled=False, axis_index_groups=ygroups
    )
    group_peak = jnp.max(jnp.abs(hidden_all)).astype(jnp.float32)
    out_cols = lax.dot_general(
        hidden_all,
        down_cols.reshape(HALVES, ys, units, cols),
        (((0, 1, 3), (1, 0, 2)), ((), ())),
        preferred_element_type=jnp.float32,
    ).astype(jnp.bfloat16)
    half_rows = lax.all_to_all(
        out_cols.reshape(ys, experts, HALVES * CAP, cols),
        "replica",
        split_axis=0,
        concat_axis=3,
        tiled=True,
        axis_index_groups=ygroups,
    )
    returned = lax.all_to_all(
        half_rows.reshape(experts, HALVES * CAP, ys * cols), "expert", 0, 0, tiled=True
    ).reshape(experts, HALVES, CAP, ys * cols)
    by_block = returned.transpose(1, 0, 2, 3).reshape(HALVES, experts * CAP, ys * cols)
    fetched = jax.vmap(lambda t, s: jnp.take(t, s, axis=0))(by_block, slot_of)
    scales = jnp.where(slot_kept, blk_gw.reshape(HALVES, -1), jnp.float32(0.0))
    combined = jnp.sum(
        (scales[..., None] * fetched).reshape(HALVES, tok_rows, TOPK, ys * cols), axis=2
    )
    own_half = jnp.where(first, combined[0], combined[1])
    send_half = jnp.where(first, combined[1], combined[0])
    recv_half = lax.ppermute(send_half, "replica", across)
    moe_output = jnp.where(
        first,
        jnp.concatenate([own_half, recv_half], axis=1),
        jnp.concatenate([recv_half, own_half], axis=1),
    ).astype(jnp.bfloat16)
    moved_gate, moved_up, moved_down = (
        jnp.where(swapped, got, own) for got, own in zip(arrived, (w_gate, w_up, w_down))
    )
    expert_peak = jnp.where(swapped, lax.ppermute(group_peak, "expert", ring), group_peak)
    return (moe_output, moved_gate, moved_up, moved_down, expert_peak.reshape(1))


def solution(mesh):
    placed = (
        P(("expert", "replica"), None),
        P(("expert", "replica"), None),
        P(("expert", "replica"), None),
        P(),
        P(),
        P(),
        P("expert", "replica", None),
        P("expert", "replica", None),
        P("expert", "replica", None),
    )
    return jax.shard_map(
        shards,
        mesh=mesh,
        in_specs=placed,
        out_specs=(
            P(("expert", "replica"), None),
            P("expert", "replica", None),
            P("expert", "replica", None),
            P("expert", "replica", None),
            P("expert"),
        ),
        check_vma=False,
    )
```

```python
import jax
import jax.numpy as jnp
from jax import lax
from jax.sharding import PartitionSpec as P

TOPK = 8
CAP = 4
HALVES = 2


def pair_partner(swap_pairs, device_count):
    devices = jnp.arange(device_count, dtype=jnp.int32)
    first_dev = swap_pairs[:, 0:1]
    second_dev = swap_pairs[:, 1:2]
    offsets = jnp.where(devices[None, :] == first_dev, second_dev - first_dev, 0)
    offsets = offsets + jnp.where(devices[None, :] == second_dev, first_dev - second_dev, 0)
    return devices + jnp.sum(offsets, axis=0)


def table_lookup(values_table, positions):
    matches = positions[..., None] == jnp.arange(values_table.shape[0], dtype=jnp.int32)
    return jnp.sum(jnp.where(matches, values_table, 0), axis=-1)


def route_slots(expert_ids, holder_now, capacity):
    expert_count = holder_now.shape[0]
    flat_ids = expert_ids.reshape(-1)
    chosen = (flat_ids[:, None] == jnp.arange(expert_count, dtype=jnp.int32)[None, :]).astype(
        jnp.int32
    )
    earlier = jnp.cumsum(chosen, axis=0) - chosen
    ranking = jnp.sum(earlier * chosen, axis=1)
    slot_kept = ranking < table_lookup(capacity, flat_ids)
    target = table_lookup(holder_now, flat_ids)
    slot_ids = jnp.where(slot_kept, target * CAP + ranking, -1)
    matched = slot_ids[None, :] == jnp.arange(expert_count * CAP, dtype=jnp.int32)[:, None]
    owners = jnp.arange(flat_ids.shape[0], dtype=jnp.int32) // TOPK
    source = jnp.sum(jnp.where(matched, owners[None, :], 0), axis=1)
    filled = jnp.any(matched, axis=1)
    return (jnp.maximum(slot_ids, 0), slot_kept, source, filled)


def expert_hidden(row_block, gate_local, up_local):
    leading = row_block.shape[:-1]
    row_matrix = row_block.reshape(-1, row_block.shape[-1])
    contract = (((1,), (1,)), ((), ()))
    gate_value = lax.dot_general(
        row_matrix, gate_local, contract, preferred_element_type=jnp.float32
    )
    up_value = lax.dot_general(row_matrix, up_local, contract, preferred_element_type=jnp.float32)
    hidden = (jax.nn.silu(gate_value) * up_value).astype(jnp.bfloat16)
    return hidden.reshape(leading + (gate_local.shape[0],))


def canonical(mine, theirs, first):
    return jnp.stack([jnp.where(first, mine, theirs), jnp.where(first, theirs, mine)])


def shards(
    tokens, expert_ids, gate_weights, expert_holder, swap_pairs, capacity, w_gate, w_up, w_down
):
    experts = lax.axis_size("expert")
    replicas = lax.axis_size("replica")
    tok_rows, width = tokens.shape
    units = w_gate.shape[1]
    ys = replicas // HALVES
    partner = pair_partner(swap_pairs, experts)
    me = lax.axis_index("expert")
    swapped = lax.dynamic_index_in_dim(partner, me, 0, keepdims=False) != me
    half = experts // 2
    ring = [(d, (d + half) % experts) for d in range(experts)]
    rep = lax.axis_index("replica")
    zh = rep // ys
    first = zh == 0
    across = [(q, (q + ys) % replicas) for q in range(replicas)]
    ygroups = [[h * ys + j for j in range(ys)] for h in range(HALVES)]
    arrived = tuple(lax.ppermute(w, "expert", ring) for w in (w_gate, w_up, w_down))
    down_cols = lax.all_to_all(
        w_down[0].reshape(units, ys, width // ys),
        "replica",
        split_axis=1,
        concat_axis=0,
        tiled=True,
        axis_index_groups=ygroups,
    ).reshape(ys, units, width // ys)
    blk_tokens = canonical(tokens, lax.ppermute(tokens, "replica", across), first)
    blk_ids = canonical(expert_ids, lax.ppermute(expert_ids, "replica", across), first)
    blk_gw = canonical(gate_weights, lax.ppermute(gate_weights, "replica", across), first)
    slot_of, slot_kept, source, filled = jax.vmap(route_slots, in_axes=(0, None, None))(
        blk_ids, expert_holder, capacity
    )
    picked = jax.vmap(lambda t, s: jnp.take(t, s, axis=0))(blk_tokens, source)
    outgoing = jnp.where(filled[..., None], picked, jnp.zeros((), jnp.bfloat16))
    outgoing = outgoing.reshape(HALVES, experts, CAP, width).transpose(1, 0, 2, 3)
    outgoing = outgoing.reshape(experts, HALVES * CAP, width)
    arrived_rows = lax.all_to_all(outgoing, "expert", 0, 0, tiled=True)
    group_rows = lax.all_gather(
        arrived_rows, "replica", axis=0, tiled=False, axis_index_groups=ygroups
    )
    hidden = expert_hidden(group_rows, w_gate[0], w_up[0]).reshape(-1, units)
    hidden_all = lax.all_gather(hidden, "replica", axis=0, tiled=False, axis_index_groups=ygroups)
    half_peak = jnp.max(jnp.abs(hidden_all)).astype(jnp.float32)
    group_peak = jnp.maximum(half_peak, lax.ppermute(half_peak, "replica", across))
    out_cols = lax.dot_general(
        hidden_all,
        down_cols,
        (((0, 2), (0, 1)), ((), ())),
        preferred_element_type=jnp.float32,
    ).astype(jnp.bfloat16)
    half_rows = lax.all_to_all(
        out_cols.reshape(ys, experts, HALVES * CAP, width // ys),
        "replica",
        split_axis=0,
        concat_axis=3,
        tiled=True,
        axis_index_groups=ygroups,
    )
    returned = lax.all_to_all(
        half_rows.reshape(experts, HALVES * CAP, width), "expert", 0, 0, tiled=True
    ).reshape(experts, HALVES, CAP, width)
    by_block = returned.transpose(1, 0, 2, 3).reshape(HALVES, experts * CAP, width)
    fetched = jax.vmap(lambda t, s: jnp.take(t, s, axis=0))(by_block, slot_of)
    scales = jnp.where(slot_kept, blk_gw.reshape(HALVES, -1), jnp.float32(0.0))
    combined = jnp.sum((scales[..., None] * fetched).reshape(HALVES, tok_rows, TOPK, width), axis=2)
    own_half = jnp.where(first, combined[0], combined[1])
    send_half = jnp.where(first, combined[1], combined[0])
    recv_half = lax.ppermute(send_half, "replica", across)
    moe_output = (own_half + recv_half).astype(jnp.bfloat16)
    moved_gate, moved_up, moved_down = (
        jnp.where(swapped, got, own) for got, own in zip(arrived, (w_gate, w_up, w_down))
    )
    expert_peak = jnp.where(swapped, lax.ppermute(group_peak, "expert", ring), group_peak)
    return (moe_output, moved_gate, moved_up, moved_down, expert_peak.reshape(1))


def solution(mesh):
    placed = (
        P(("expert", "replica"), None),
        P(("expert", "replica"), None),
        P(("expert", "replica"), None),
        P(),
        P(),
        P(),
        P("expert", "replica", None),
        P("expert", "replica", None),
        P("expert", "replica", None),
    )
    return jax.shard_map(
        shards,
        mesh=mesh,
        in_specs=placed,
        out_specs=(
            P(("expert", "replica"), None),
            P("expert", "replica", None),
            P("expert", "replica", None),
            P("expert", "replica", None),
            P("expert"),
        ),
        check_vma=False,
    )
```
